32 devices in a mesh: group: 2 (over x), seq: 16 (over z, y, core).
Axes of the slice: x: 2, y: 2, z: 4, core: 2. Of those that a mesh axis runs over, the one named last changes fastest.
Arguments:
- queries: bfloat16 [4, 2048, 4096], P('group', 'seq'), parts along dimension 0, may hold values from -32 to 32
- key_vectors: bfloat16 [4, 2048, 4096], P('group', 'seq'), parts along dimension 0, may hold values from -24 to 24
- value_vectors: bfloat16 [4, 2048, 4096], P('group', 'seq'), parts along dimension 0, may hold values from -6 to 6
- out_grad: bfloat16 [4, 2048, 4096], P('group', 'seq'), parts along dimension 0, may hold values from -6 to 6
Outputs:
- grad_queries: bfloat16 [4, 2048, 4096], P('group', 'seq'), parts along dimension 0
- grad_keys: bfloat16 [4, 2048, 4096], P('group', 'seq'), parts along dimension 0
- grad_values: bfloat16 [4, 2048, 4096], P('group', 'seq'), parts along dimension 0
The draws below stay inside these ranges and needn't reach their ends.
There are 2 independent parts, one for each index of `group`. The reference program is written for one: setup_inputs(seed, part) draws one part's arguments, and reference() takes and returns one part's arrays. A program takes and returns all parts, laid end to end along the dimension named above; each array names one. Nothing has to cross between parts.
All inputs are finite; a program needn't handle non-finite values.
Results may differ from the reference program's by a relative error of at most 0.0052.
Values may be sent and summed in bfloat16 or wider, within the bound.
No kernel may reach another device: no remote copies, remote signals or barrier semaphores. Data moves between devices by JAX's collectives and lax.ppermute only.
A program may use at most 128 MiB of HBM per device.

```python
import jax
import jax.numpy as jnp
from jax import lax

HEADS = 32
HEAD_DIM = 128
PAGES = 2
TOKENS = 2048


def draw_pair(key):
    base_key = jax.random.fold_in(key, 4099)
    key_query, key_keys = jax.random.split(base_key, 2)
    feature_width = HEADS * HEAD_DIM
    queries = jnp.clip(jax.random.normal(key_query, (PAGES, TOKENS, feature_width), jnp.float32), -6.0, 6.0)
    key_vectors = jnp.clip(jax.random.normal(key_keys, (PAGES, TOKENS, feature_width), jnp.float32), -6.0, 6.0)
    return (queries, key_vectors)


def draw_queries(key, part):
    return draw_pair(key)[0].astype(jnp.bfloat16)


def draw_key_vectors(key, part):
    return draw_pair(key)[1].astype(jnp.bfloat16)


def steps_of(stream_key, dims, cuts, low, high):
    def one(position, parts):
        heights = jax.random.uniform(jax.random.fold_in(jax.random.fold_in(stream_key, 6), position), (parts,), jnp.float32, low / len(cuts), high / len(cuts))
        return jnp.repeat(jnp.exp(heights), dims[position] // parts).reshape((-1,) + (1,) * (len(dims) - position - 1))

    gain = one(*cuts[0])
    for cut in cuts[1:]:
        gain = gain * one(*cut)
    return gain


def gaussian(key, extent, deviation, reach, cuts=(), kind=jnp.bfloat16):
    entries = deviation * jax.random.normal(key, extent, jnp.float32)
    if cuts:
        entries = entries * steps_of(key, extent, cuts, -0.22, 0.18)
    return jnp.clip(entries, -reach, reach).astype(kind)


def setup_inputs(seed: int = 0, part: int = 0) -> dict:
    splits = jax.random.split(jax.random.key(seed), 5)
    own_keys = jax.random.split(jax.random.fold_in(splits[4], part), 5)
    queries = draw_queries(jax.random.fold_in(jax.random.fold_in(splits[4], part), 71), part)
    key_vectors = draw_key_vectors(jax.random.fold_in(jax.random.fold_in(splits[4], part), 71), part)
    value_vectors = gaussian(own_keys[2], (PAGES, TOKENS, HEADS * HEAD_DIM), 1.0, 6.0, ((1, 16),))
    out_grad = gaussian(own_keys[3], (PAGES, TOKENS, HEADS * HEAD_DIM), 1.0, 6.0, ((1, 16),))
    return {"queries": queries, "key_vectors": key_vectors, "value_vectors": value_vectors, "out_grad": out_grad}


def single_head(operands):
    queries, key_vectors, value_vectors, out_grad = operands
    tokens_all = queries.shape[0]
    score_scale = queries.shape[1] ** -0.5
    scores = jnp.dot(queries, key_vectors.T, preferred_element_type=jnp.float32) * score_scale
    positions = jnp.arange(tokens_all, dtype=jnp.int32)
    causal_mask = positions[:, None] >= positions[None, :]
    scores = jnp.where(causal_mask, scores, -jnp.inf)
    row_top = jnp.max(scores, axis=1, keepdims=True)
    weights = jnp.exp(scores - row_top)
    softmax_rows = weights / jnp.sum(weights, axis=1, keepdims=True)
    probs_low = softmax_rows.astype(jnp.bfloat16)
    dprobs = jnp.dot(out_grad, value_vectors.T, preferred_element_type=jnp.float32)
    row_delta = jnp.sum(softmax_rows * dprobs, axis=1, keepdims=True)
    dscores = (softmax_rows * (dprobs - row_delta)).astype(jnp.bfloat16)
    grad_values = jnp.dot(probs_low.T, out_grad, preferred_element_type=jnp.float32).astype(jnp.bfloat16)
    grad_queries = (jnp.dot(dscores, key_vectors, preferred_element_type=jnp.float32) * score_scale).astype(jnp.bfloat16)
    grad_keys = (jnp.dot(dscores.T, queries, preferred_element_type=jnp.float32) * score_scale).astype(jnp.bfloat16)
    return grad_queries, grad_keys, grad_values


def to_heads(operand):
    shaped = operand.reshape(PAGES, TOKENS, HEADS, HEAD_DIM).transpose(0, 2, 1, 3)
    return shaped.reshape(PAGES * HEADS, TOKENS, HEAD_DIM)


def to_tokens(operand):
    shaped = operand.reshape(PAGES, HEADS, TOKENS, HEAD_DIM).transpose(0, 2, 1, 3)
    return shaped.reshape(PAGES, TOKENS, HEADS * HEAD_DIM)


def reference(queries, key_vectors, value_vectors, out_grad):
    gradients = lax.map(single_head, (to_heads(queries), to_heads(key_vectors), to_heads(value_vectors), to_heads(out_grad)))
    return (to_tokens(gradients[0]), to_tokens(gradients[1]), to_tokens(gradients[2]))
```

```python
import jax
import jax.numpy as jnp
from jax import lax
from jax.sharding import PartitionSpec as P

HEADS = 32


def item_gradients(queries, key_vectors, value_vectors, out_grad):
    tokens_all, head_width = queries.shape
    score_scale = head_width ** (-0.5)
    block_rows = min(512, tokens_all)
    grad_keys = jnp.zeros((tokens_all, head_width), jnp.float32)
    grad_values = jnp.zeros((tokens_all, head_width), jnp.float32)
    query_parts = []
    for block_index in range(tokens_all // block_rows):
        row_start = block_index * block_rows
        row_stop = row_start + block_rows
        query_block = queries[row_start:row_stop]
        grad_block = out_grad[row_start:row_stop]
        key_prefix = key_vectors[:row_stop]
        value_prefix = value_vectors[:row_stop]
        scores = (
            jnp.dot(query_block, key_prefix.T, preferred_element_type=jnp.float32) * score_scale
        )
        row_ids = row_start + lax.broadcasted_iota(jnp.int32, (block_rows, row_stop), 0)
        col_ids = lax.broadcasted_iota(jnp.int32, (block_rows, row_stop), 1)
        scores = jnp.where(row_ids >= col_ids, scores, -jnp.inf)
        row_top = jnp.max(scores, axis=1, keepdims=True)
        weights = jnp.exp(scores - row_top)
        softmax_rows = weights / jnp.sum(weights, axis=1, keepdims=True)
        probs_low = softmax_rows.astype(jnp.bfloat16)
        dprobs = jnp.dot(grad_block, value_prefix.T, preferred_element_type=jnp.float32)
        row_delta = jnp.sum(softmax_rows * dprobs, axis=1, keepdims=True)
        dscores = (softmax_rows * (dprobs - row_delta)).astype(jnp.bfloat16)
        value_terms = jnp.dot(probs_low.T, grad_block, preferred_element_type=jnp.float32)
        grad_values = grad_values.at[:row_stop].add(value_terms)
        key_terms = (
            jnp.dot(dscores.T, query_block, preferred_element_type=jnp.float32) * score_scale
        )
        grad_keys = grad_keys.at[:row_stop].add(key_terms)
        query_terms = jnp.dot(dscores, key_prefix, preferred_element_type=jnp.float32) * score_scale
        query_parts.append(query_terms.astype(jnp.bfloat16))
    grad_queries = jnp.concatenate(query_parts, axis=0)
    return grad_queries, grad_keys.astype(jnp.bfloat16), grad_values.astype(jnp.bfloat16)


def body(queries, key_vectors, value_vectors, out_grad):
    page_count, tok_rows, feature_width = queries.shape
    seq_size = lax.psum(1, "seq")
    head_width = feature_width // HEADS
    per_dev = HEADS // seq_size
    stacked = jnp.stack([queries, key_vectors, value_vectors, out_grad]).reshape(
        4, page_count, tok_rows, seq_size, per_dev, head_width
    )
    chunk_out = {}
    for page in range(page_count):
        for head in range(per_dev):
            part = stacked[:, page, :, :, head, :]
            arrived = lax.all_to_all(part, "seq", split_axis=2, concat_axis=1, tiled=True)
            arrived = arrived.reshape(4, seq_size * tok_rows, head_width)
            grads = item_gradients(arrived[0], arrived[1], arrived[2], arrived[3])
            grads = jnp.stack(grads).reshape(3, seq_size, tok_rows, 1, head_width)
            returned = lax.all_to_all(grads, "seq", split_axis=1, concat_axis=3, tiled=True)
            chunk_out[(page, head)] = returned.reshape(3, tok_rows, seq_size, head_width)
    pages = []
    for page in range(page_count):
        pages.append(jnp.stack([chunk_out[(page, head)] for head in range(per_dev)], axis=3))
    result = jnp.stack(pages, axis=1).reshape(3, page_count, tok_rows, feature_width)
    return result[0], result[1], result[2]


def solution(mesh):
    placed = P("group", "seq", None)
    return jax.shard_map(
        body,
        mesh=mesh,
        in_specs=(placed, placed, placed, placed),
        out_specs=(placed, placed, placed),
        check_vma=False,
    )
```

```python
import jax
import jax.numpy as jnp
from jax import lax
from jax.sharding import PartitionSpec as P

HEADS = 32


def item_gradients(queries, key_vectors, value_vectors, out_grad):
    tokens_all, head_width = queries.shape
    score_scale = head_width ** (-0.5)
    block_rows = min(512, tokens_all)
    grad_keys = jnp.zeros((tokens_all, head_width), jnp.float32)
    grad_values = jnp.zeros((tokens_all, head_width), jnp.float32)
    query_parts = []
    for block_index in range(tokens_all // block_rows):
        row_start = block_index * block_rows
        row_stop = row_start + block_rows
        query_block = queries[row_start:row_stop]
        grad_block = out_grad[row_start:row_stop]
        key_prefix = key_vectors[:row_stop]
        value_prefix = value_vectors[:row_stop]
        scores = (
            jnp.dot(query_block, key_prefix.T, preferred_element_type=jnp.float32) * score_scale
        )
        row_ids = row_start + lax.broadcasted_iota(jnp.int32, (block_rows, row_stop), 0)
        col_ids = lax.broadcasted_iota(jnp.int32, (block_rows, row_stop), 1)
        scores = jnp.where(row_ids >= col_ids, scores, -jnp.inf)
        row_top = jnp.max(scores, axis=1, keepdims=True)
        weights = jnp.exp(scores - row_top)
        softmax_rows = weights / jnp.sum(weights, axis=1, keepdims=True)
        probs_low = softmax_rows.astype(jnp.bfloat16)
        dprobs = jnp.dot(grad_block, value_prefix.T, preferred_element_type=jnp.float32)
        row_delta = jnp.sum(softmax_rows * dprobs, axis=1, keepdims=True)
        dscores = (softmax_rows * (dprobs - row_delta)).astype(jnp.bfloat16)
        value_terms = jnp.dot(probs_low.T, grad_block, preferred_element_type=jnp.float32)
        grad_values = grad_values.at[:row_stop].add(value_terms)
        key_terms = (
            jnp.dot(dscores.T, query_block, preferred_element_type=jnp.float32) * score_scale
        )
        grad_keys = grad_keys.at[:row_stop].add(key_terms)
        query_terms = jnp.dot(dscores, key_prefix, preferred_element_type=jnp.float32) * score_scale
        query_parts.append(query_terms.astype(jnp.bfloat16))
    grad_queries = jnp.concatenate(query_parts, axis=0)
    return grad_queries, grad_keys.astype(jnp.bfloat16), grad_values.astype(jnp.bfloat16)


def body(queries, key_vectors, value_vectors, out_grad):
    page_count, tok_rows, feature_width = queries.shape
    seq_size = lax.psum(1, "seq")
    head_width = feature_width // HEADS
    per_dev = HEADS // seq_size
    chunks = page_count * per_dev
    tokens_all = seq_size * tok_rows
    stacked = jnp.stack([queries, key_vectors, value_vectors, out_grad]).reshape(
        4, page_count, tok_rows, seq_size, per_dev, head_width
    )
    stacked = stacked.transpose(1, 4, 0, 2, 3, 5).reshape(chunks, 4, tok_rows, seq_size, head_width)

    def fetch(chunk):
        part = lax.dynamic_index_in_dim(stacked, chunk, 0, keepdims=False)
        arrived = lax.all_to_all(part, "seq", split_axis=2, concat_axis=1, tiled=True)
        return arrived.reshape(4, tokens_all, head_width)

    def compute(arrived):
        grads = item_gradients(arrived[0], arrived[1], arrived[2], arrived[3])
        return jnp.stack(grads).reshape(3, seq_size, tok_rows, 1, head_width)

    def send(grads, out_buf, chunk):
        returned = lax.all_to_all(grads, "seq", split_axis=1, concat_axis=3, tiled=True)
        returned = returned.reshape(1, 3, tok_rows, seq_size, head_width)
        return lax.dynamic_update_index_in_dim(out_buf, returned[0], chunk, 0)

    out_buf = jnp.zeros((chunks, 3, tok_rows, seq_size, head_width), jnp.bfloat16)
    current = fetch(0)
    if chunks > 1:
        upcoming = fetch(1)
        prev = compute(current)
        current = upcoming

        def loop_body(chunk, carry):
            current, prev, out_buf = carry
            upcoming = fetch(chunk + 1)
            grads = compute(current)
            out_buf = send(prev, out_buf, chunk - 1)
            return upcoming, grads, out_buf

        current, prev, out_buf = lax.fori_loop(1, chunks - 1, loop_body, (current, prev, out_buf))
        last = compute(current)
        out_buf = send(prev, out_buf, chunks - 2)
        out_buf = send(last, out_buf, chunks - 1)
    else:
        out_buf = send(compute(current), out_buf, 0)
    result = out_buf.reshape(page_count, per_dev, 3, tok_rows, seq_size, head_width)
    result = result.transpose(2, 0, 3, 4, 1, 5).reshape(3, page_count, tok_rows, feature_width)
    return result[0], result[1], result[2]


def solution(mesh):
    placed = P("group", "seq", None)
    return jax.shard_map(
        body,
        mesh=mesh,
        in_specs=(placed, placed, placed, placed),
        out_specs=(placed, placed, placed),
        check_vma=False,
    )
```

```python
import jax
import jax.numpy as jnp
from jax import lax
from jax.experimental import pallas as pl
from jax.experimental.pallas import tpu as pltpu
from jax.sharding import PartitionSpec as P

HEADS = 32
BLOCK = 256


def _kernel(q_ref, k_ref, v_ref, do_ref, dq_ref, dk_ref, dv_ref, s_scr, dp_scr, dk_acc, dv_acc):
    tokens_all, head_width = q_ref.shape
    blk = BLOCK
    scale = head_width ** (-0.5)
    dk_acc[...] = jnp.zeros_like(dk_acc)
    dv_acc[...] = jnp.zeros_like(dv_acc)
    contract_rows = (((0,), (0,)), ((), ()))
    contract_cols = (((1,), (1,)), ((), ()))

    def row_block(i, carry):
        r0 = pl.multiple_of(i * blk, blk)
        q = q_ref[pl.ds(r0, blk), :]
        do = do_ref[pl.ds(r0, blk), :]
        count = i + 1

        def scores_pass(j, top):
            c0 = pl.multiple_of(j * blk, blk)
            s = lax.dot_general(q, k_ref[pl.ds(c0, blk), :], contract_cols,
                                preferred_element_type=jnp.float32) * scale
            rows = r0 + lax.broadcasted_iota(jnp.int32, (blk, blk), 0)
            cols = c0 + lax.broadcasted_iota(jnp.int32, (blk, blk), 1)
            s = jnp.where(rows >= cols, s, -jnp.inf)
            s_scr[:, pl.ds(c0, blk)] = s
            return jnp.maximum(top, jnp.max(s, axis=1, keepdims=True))

        top = lax.fori_loop(0, count, scores_pass, jnp.full((blk, 1), -jnp.inf, jnp.float32))

        def weights_pass(j, total):
            c0 = pl.multiple_of(j * blk, blk)
            w = jnp.exp(s_scr[:, pl.ds(c0, blk)] - top)
            s_scr[:, pl.ds(c0, blk)] = w
            return total + jnp.sum(w, axis=1, keepdims=True)

        total = lax.fori_loop(0, count, weights_pass, jnp.zeros((blk, 1), jnp.float32))

        def probs_pass(j, delta):
            c0 = pl.multiple_of(j * blk, blk)
            p = s_scr[:, pl.ds(c0, blk)] / total
            dp = lax.dot_general(do, v_ref[pl.ds(c0, blk), :], contract_cols,
                                 preferred_element_type=jnp.float32)
            s_scr[:, pl.ds(c0, blk)] = p
            dp_scr[:, pl.ds(c0, blk)] = dp
            return delta + jnp.sum(p * dp, axis=1, keepdims=True)

        delta = lax.fori_loop(0, count, probs_pass, jnp.zeros((blk, 1), jnp.float32))

        def grads_pass(j, dq):
            c0 = pl.multiple_of(j * blk, blk)
            p = s_scr[:, pl.ds(c0, blk)]
            ds = (p * (dp_scr[:, pl.ds(c0, blk)] - delta)).astype(jnp.bfloat16)
            dq = dq + jnp.dot(ds, k_ref[pl.ds(c0, blk), :], preferred_element_type=jnp.float32)
            dk_acc[pl.ds(c0, blk), :] += lax.dot_general(
                ds, q, contract_rows, preferred_element_type=jnp.float32)
            dv_acc[pl.ds(c0, blk), :] += lax.dot_general(
                p.astype(jnp.bfloat16), do, contract_rows, preferred_element_type=jnp.float32)
            return dq

        dq = lax.fori_loop(0, count, grads_pass, jnp.zeros((blk, head_width), jnp.float32))
        dq_ref[pl.ds(r0, blk), :] = (dq * scale).astype(dq_ref.dtype)
        return carry

    lax.fori_loop(0, tokens_all // blk, row_block, 0)
    dk_ref[...] = (dk_acc[...] * scale).astype(dk_ref.dtype)
    dv_ref[...] = dv_acc[...].astype(dv_ref.dtype)


def item_gradients(queries, key_vectors, value_vectors, out_grad):
    tokens_all, head_width = queries.shape
    out = jax.ShapeDtypeStruct((tokens_all, head_width), jnp.bfloat16)
    return pl.pallas_call(
        _kernel,
        out_shape=(out, out, out),
        scratch_shapes=[
            pltpu.VMEM((BLOCK, tokens_all), jnp.float32),
            pltpu.VMEM((BLOCK, tokens_all), jnp.float32),
            pltpu.VMEM((tokens_all, head_width), jnp.float32),
            pltpu.VMEM((tokens_all, head_width), jnp.float32),
        ],
        compiler_params=pltpu.CompilerParams(vmem_limit_bytes=32 * 1024 * 1024),
    )(queries, key_vectors, value_vectors, out_grad)


def body(queries, key_vectors, value_vectors, out_grad):
    page_count, tok_rows, feature_width = queries.shape
    seq_size = lax.psum(1, "seq")
    head_width = feature_width // HEADS
    per_dev = HEADS // seq_size
    stacked = jnp.stack([queries, key_vectors, value_vectors, out_grad]).reshape(
        4, page_count, tok_rows, seq_size, per_dev, head_width
    )
    chunk_out = {}
    for page in range(page_count):
        for head in range(per_dev):
            part = stacked[:, page, :, :, head, :]
            arrived = lax.all_to_all(part, "seq", split_axis=2, concat_axis=1, tiled=True)
            arrived = arrived.reshape(4, seq_size * tok_rows, head_width)
            grads = item_gradients(arrived[0], arrived[1], arrived[2], arrived[3])
            grads = jnp.stack(grads).reshape(3, seq_size, tok_rows, 1, head_width)
            returned = lax.all_to_all(grads, "seq", split_axis=1, concat_axis=3, tiled=True)
            chunk_out[(page, head)] = returned.reshape(3, tok_rows, seq_size, head_width)
    pages = []
    for page in range(page_count):
        pages.append(jnp.stack([chunk_out[(page, head)] for head in range(per_dev)], axis=3))
    result = jnp.stack(pages, axis=1).reshape(3, page_count, tok_rows, feature_width)
    return result[0], result[1], result[2]


def solution(mesh):
    placed = P("group", "seq", None)
    return jax.shard_map(
        body,
        mesh=mesh,
        in_specs=(placed, placed, placed, placed),
        out_specs=(placed, placed, placed),
        check_vma=False,
    )
```

```python
import jax
import jax.numpy as jnp
from jax import lax
from jax.experimental import pallas as pl
from jax.experimental.pallas import tpu as pltpu
from jax.sharding import PartitionSpec as P

HEADS = 32
BLOCK = 256


def _kernel(q_ref, k_ref, v_ref, do_ref, dq_ref, dk_ref, dv_ref, s_scr, dp_scr, dk_acc, dv_acc):
    tokens_all, head_width = q_ref.shape
    blk = BLOCK
    scale = head_width ** (-0.5)
    dk_acc[...] = jnp.zeros_like(dk_acc)
    dv_acc[...] = jnp.zeros_like(dv_acc)
    contract_rows = (((0,), (0,)), ((), ()))
    contract_cols = (((1,), (1,)), ((), ()))

    def row_block(i, carry):
        r0 = pl.multiple_of(i * blk, blk)
        q = q_ref[pl.ds(r0, blk), :]
        do = do_ref[pl.ds(r0, blk), :]
        count = i + 1

        def scores_pass(j, top):
            c0 = pl.multiple_of(j * blk, blk)
            s = lax.dot_general(q, k_ref[pl.ds(c0, blk), :], contract_cols,
                                preferred_element_type=jnp.float32) * scale
            rows = r0 + lax.broadcasted_iota(jnp.int32, (blk, blk), 0)
            cols = c0 + lax.broadcasted_iota(jnp.int32, (blk, blk), 1)
            s = jnp.where(rows >= cols, s, -jnp.inf)
            s_scr[:, pl.ds(c0, blk)] = s
            return jnp.maximum(top, jnp.max(s, axis=1, keepdims=True))

        top = lax.fori_loop(0, count, scores_pass, jnp.full((blk, 1), -jnp.inf, jnp.float32))

        def weights_pass(j, total):
            c0 = pl.multiple_of(j * blk, blk)
            w = jnp.exp(s_scr[:, pl.ds(c0, blk)] - top)
            s_scr[:, pl.ds(c0, blk)] = w
            return total + jnp.sum(w, axis=1, keepdims=True)

        total = lax.fori_loop(0, count, weights_pass, jnp.zeros((blk, 1), jnp.float32))

        def probs_pass(j, delta):
            c0 = pl.multiple_of(j * blk, blk)
            p = s_scr[:, pl.ds(c0, blk)] / total
            dp = lax.dot_general(do, v_ref[pl.ds(c0, blk), :], contract_cols,
                                 preferred_element_type=jnp.float32)
            s_scr[:, pl.ds(c0, blk)] = p
            dp_scr[:, pl.ds(c0, blk)] = dp
            return delta + jnp.sum(p * dp, axis=1, keepdims=True)

        delta = lax.fori_loop(0, count, probs_pass, jnp.zeros((blk, 1), jnp.float32))

        def grads_pass(j, dq):
            c0 = pl.multiple_of(j * blk, blk)
            p = s_scr[:, pl.ds(c0, blk)]
            ds = (p * (dp_scr[:, pl.ds(c0, blk)] - delta)).astype(jnp.bfloat16)
            dq = dq + jnp.dot(ds, k_ref[pl.ds(c0, blk), :], preferred_element_type=jnp.float32)
            dk_acc[pl.ds(c0, blk), :] += lax.dot_general(
                ds, q, contract_rows, preferred_element_type=jnp.float32)
            dv_acc[pl.ds(c0, blk), :] += lax.dot_general(
                p.astype(jnp.bfloat16), do, contract_rows, preferred_element_type=jnp.float32)
            return dq

        dq = lax.fori_loop(0, count, grads_pass, jnp.zeros((blk, head_width), jnp.float32))
        dq_ref[pl.ds(r0, blk), :] = (dq * scale).astype(dq_ref.dtype)
        return carry

    lax.fori_loop(0, tokens_all // blk, row_block, 0)
    dk_ref[...] = (dk_acc[...] * scale).astype(dk_ref.dtype)
    dv_ref[...] = dv_acc[...].astype(dv_ref.dtype)


def item_gradients(queries, key_vectors, value_vectors, out_grad):
    tokens_all, head_width = queries.shape
    out = jax.ShapeDtypeStruct((tokens_all, head_width), jnp.bfloat16)
    return pl.pallas_call(
        _kernel,
        out_shape=(out, out, out),
        scratch_shapes=[
            pltpu.VMEM((BLOCK, tokens_all), jnp.float32),
            pltpu.VMEM((BLOCK, tokens_all), jnp.float32),
            pltpu.VMEM((tokens_all, head_width), jnp.float32),
            pltpu.VMEM((tokens_all, head_width), jnp.float32),
        ],
        compiler_params=pltpu.CompilerParams(vmem_limit_bytes=32 * 1024 * 1024),
    )(queries, key_vectors, value_vectors, out_grad)


def body(queries, key_vectors, value_vectors, out_grad):
    page_count, tok_rows, feature_width = queries.shape
    seq_size = lax.psum(1, "seq")
    head_width = feature_width // HEADS
    per_dev = HEADS // seq_size
    tokens_all = seq_size * tok_rows
    inputs = (queries, key_vectors, value_vectors, out_grad)
    outs = []
    for page in range(page_count):
        part = jnp.stack(
            [x[page].reshape(tok_rows, seq_size, per_dev, head_width) for x in inputs]
        ).transpose(2, 0, 1, 3, 4)
        arrived = lax.all_to_all(part, "seq", split_axis=0, concat_axis=0, tiled=True)
        arrived = arrived.reshape(seq_size, 4, tok_rows, per_dev, head_width)
        grads = []
        for head in range(per_dev):
            items = [
                arrived[:, a, :, head, :].reshape(tokens_all, head_width) for a in range(4)
            ]
            grads.append(jnp.stack(item_gradients(*items)))
        grads = jnp.stack(grads).reshape(per_dev, 3, seq_size, tok_rows, head_width)
        grads = grads.transpose(2, 1, 0, 3, 4)
        returned = lax.all_to_all(grads, "seq", split_axis=0, concat_axis=0, tiled=True)
        outs.append(returned.transpose(1, 3, 0, 2, 4).reshape(3, tok_rows, feature_width))
    result = jnp.stack(outs, axis=1)
    return result[0], result[1], result[2]


def solution(mesh):
    placed = P("group", "seq", None)
    return jax.shard_map(
        body,
        mesh=mesh,
        in_specs=(placed, placed, placed, placed),
        out_specs=(placed, placed, placed),
        check_vma=False,
    )
```

```python
import jax
import jax.numpy as jnp
from jax import lax
from jax.experimental import pallas as pl
from jax.experimental.pallas import tpu as pltpu
from jax.sharding import PartitionSpec as P

HEADS = 32
BLOCK = 256


def _kernel(q_ref, k_ref, v_ref, do_ref, dq_ref, dk_ref, dv_ref, s_scr, dp_scr, dk_acc, dv_acc):
    tokens_all, head_width = q_ref.shape
    blk = BLOCK
    scale = head_width ** (-0.5)
    dk_acc[...] = jnp.zeros_like(dk_acc)
    dv_acc[...] = jnp.zeros_like(dv_acc)
    contract_rows = (((0,), (0,)), ((), ()))
    contract_cols = (((1,), (1,)), ((), ()))
    row_ids = lax.broadcasted_iota(jnp.int32, (blk, blk), 0)
    col_ids = lax.broadcasted_iota(jnp.int32, (blk, blk), 1)

    def row_block(i, carry):
        r0 = pl.multiple_of(i * blk, blk)
        q = q_ref[pl.ds(r0, blk), :]
        do = do_ref[pl.ds(r0, blk), :]

        def scores(j, masked):
            c0 = pl.multiple_of(j * blk, blk)
            s = lax.dot_general(q, k_ref[pl.ds(c0, blk), :], contract_cols,
                                preferred_element_type=jnp.float32) * scale
            if masked:
                s = jnp.where(row_ids >= col_ids, s, -jnp.inf)
            s_scr[:, pl.ds(c0, blk)] = s
            return jnp.max(s, axis=1, keepdims=True)

        top = lax.fori_loop(
            0, i, lambda j, t: jnp.maximum(t, scores(j, False)),
            jnp.full((blk, 1), -jnp.inf, jnp.float32))
        top = jnp.maximum(top, scores(i, True))

        def weights_pass(j, sums):
            total, weighted = sums
            c0 = pl.multiple_of(j * blk, blk)
            w = jnp.exp(s_scr[:, pl.ds(c0, blk)] - top)
            dp = lax.dot_general(do, v_ref[pl.ds(c0, blk), :], contract_cols,
                                 preferred_element_type=jnp.float32)
            s_scr[:, pl.ds(c0, blk)] = w
            dp_scr[:, pl.ds(c0, blk)] = dp
            return (total + jnp.sum(w, axis=1, keepdims=True),
                    weighted + jnp.sum(w * dp, axis=1, keepdims=True))

        zero_col = jnp.zeros((blk, 1), jnp.float32)
        total, weighted = lax.fori_loop(0, i + 1, weights_pass, (zero_col, zero_col))
        inv_total = 1.0 / total
        delta = weighted * inv_total

        def grads_pass(j, dq):
            c0 = pl.multiple_of(j * blk, blk)
            p = s_scr[:, pl.ds(c0, blk)] * inv_total
            ds = (p * (dp_scr[:, pl.ds(c0, blk)] - delta)).astype(jnp.bfloat16)
            dq = dq + jnp.dot(ds, k_ref[pl.ds(c0, blk), :], preferred_element_type=jnp.float32)
            dk_acc[pl.ds(c0, blk), :] += lax.dot_general(
                ds, q, contract_rows, preferred_element_type=jnp.float32)
            dv_acc[pl.ds(c0, blk), :] += lax.dot_general(
                p.astype(jnp.bfloat16), do, contract_rows, preferred_element_type=jnp.float32)
            return dq

        dq = lax.fori_loop(0, i + 1, grads_pass, jnp.zeros((blk, head_width), jnp.float32))
        dq_ref[pl.ds(r0, blk), :] = (dq * scale).astype(dq_ref.dtype)
        return carry

    lax.fori_loop(0, tokens_all // blk, row_block, 0)
    dk_ref[...] = (dk_acc[...] * scale).astype(dk_ref.dtype)
    dv_ref[...] = dv_acc[...].astype(dv_ref.dtype)


def item_gradients(queries, key_vectors, value_vectors, out_grad):
    tokens_all, head_width = queries.shape
    out = jax.ShapeDtypeStruct((tokens_all, head_width), jnp.bfloat16)
    return pl.pallas_call(
        _kernel,
        out_shape=(out, out, out),
        scratch_shapes=[
            pltpu.VMEM((BLOCK, tokens_all), jnp.float32),
            pltpu.VMEM((BLOCK, tokens_all), jnp.float32),
            pltpu.VMEM((tokens_all, head_width), jnp.float32),
            pltpu.VMEM((tokens_all, head_width), jnp.float32),
        ],
        compiler_params=pltpu.CompilerParams(vmem_limit_bytes=32 * 1024 * 1024),
    )(queries, key_vectors, value_vectors, out_grad)


def body(queries, key_vectors, value_vectors, out_grad):
    page_count, tok_rows, feature_width = queries.shape
    seq_size = lax.psum(1, "seq")
    head_width = feature_width // HEADS
    per_dev = HEADS // seq_size
    tokens_all = seq_size * tok_rows
    inputs = (queries, key_vectors, value_vectors, out_grad)
    outs = []
    for page in range(page_count):
        part = jnp.stack(
            [x[page].reshape(tok_rows, seq_size, per_dev, head_width) for x in inputs]
        ).transpose(2, 0, 1, 3, 4)
        arrived = lax.all_to_all(part, "seq", split_axis=0, concat_axis=0, tiled=True)
        arrived = arrived.reshape(seq_size, 4, tok_rows, per_dev, head_width)
        grads = []
        for head in range(per_dev):
            items = [
                arrived[:, a, :, head, :].reshape(tokens_all, head_width) for a in range(4)
            ]
            grads.append(jnp.stack(item_gradients(*items)))
        grads = jnp.stack(grads).reshape(per_dev, 3, seq_size, tok_rows, head_width)
        grads = grads.transpose(2, 1, 0, 3, 4)
        returned = lax.all_to_all(grads, "seq", split_axis=0, concat_axis=0, tiled=True)
        outs.append(returned.transpose(1, 3, 0, 2, 4).reshape(3, tok_rows, feature_width))
    result = jnp.stack(outs, axis=1)
    return result[0], result[1], result[2]


def solution(mesh):
    placed = P("group", "seq", None)
    return jax.shard_map(
        body,
        mesh=mesh,
        in_specs=(placed, placed, placed, placed),
        out_specs=(placed, placed, placed),
        check_vma=False,
    )
```

```python
import jax
import jax.numpy as jnp
from jax import lax
from jax.experimental import pallas as pl
from jax.experimental.pallas import tpu as pltpu
from jax.sharding import PartitionSpec as P

HEADS = 32
BLOCK = 256


def _kernel(q_ref, k_ref, kt_ref, v_ref, do_ref, dqt_ref, dk_ref, dv_ref, s_scr, dp_scr, dk_acc, dv_acc):
    tokens_all, head_width = q_ref.shape
    blk = BLOCK
    scale = head_width ** (-0.5)
    dk_acc[...] = jnp.zeros_like(dk_acc)
    dv_acc[...] = jnp.zeros_like(dv_acc)
    contract_cols = (((1,), (1,)), ((), ()))
    key_ids = lax.broadcasted_iota(jnp.int32, (blk, blk), 0)
    query_ids = lax.broadcasted_iota(jnp.int32, (blk, blk), 1)

    def query_block(i, carry):
        r0 = pl.multiple_of(i * blk, blk)
        q = q_ref[pl.ds(r0, blk), :]
        do = do_ref[pl.ds(r0, blk), :]

        def scores(j, masked):
            c0 = pl.multiple_of(j * blk, blk)
            s = lax.dot_general(k_ref[pl.ds(c0, blk), :], q, contract_cols,
                                preferred_element_type=jnp.float32) * scale
            if masked:
                s = jnp.where(query_ids >= key_ids, s, -jnp.inf)
            s_scr[pl.ds(c0, blk), :] = s
            return jnp.max(s, axis=0, keepdims=True)

        top = lax.fori_loop(
            0, i, lambda j, t: jnp.maximum(t, scores(j, False)),
            jnp.full((1, blk), -jnp.inf, jnp.float32))
        top = jnp.maximum(top, scores(i, True))

        def weights_pass(j, sums):
            total, weighted = sums
            c0 = pl.multiple_of(j * blk, blk)
            w = jnp.exp(s_scr[pl.ds(c0, blk), :] - top)
            dp = lax.dot_general(v_ref[pl.ds(c0, blk), :], do, contract_cols,
                                 preferred_element_type=jnp.float32)
            s_scr[pl.ds(c0, blk), :] = w
            dp_scr[pl.ds(c0, blk), :] = dp
            return (total + jnp.sum(w, axis=0, keepdims=True),
                    weighted + jnp.sum(w * dp, axis=0, keepdims=True))

        zero_row = jnp.zeros((1, blk), jnp.float32)
        total, weighted = lax.fori_loop(0, i + 1, weights_pass, (zero_row, zero_row))
        inv_total = 1.0 / total
        delta = weighted * inv_total

        def grads_pass(j, dqt):
            c0 = pl.multiple_of(j * blk, blk)
            p = s_scr[pl.ds(c0, blk), :] * inv_total
            ds = (p * (dp_scr[pl.ds(c0, blk), :] - delta)).astype(jnp.bfloat16)
            dqt = dqt + jnp.dot(kt_ref[:, pl.ds(c0, blk)], ds, preferred_element_type=jnp.float32)
            dk_acc[pl.ds(c0, blk), :] += jnp.dot(ds, q, preferred_element_type=jnp.float32)
            dv_acc[pl.ds(c0, blk), :] += jnp.dot(
                p.astype(jnp.bfloat16), do, preferred_element_type=jnp.float32)
            return dqt

        dqt = lax.fori_loop(0, i + 1, grads_pass, jnp.zeros((head_width, blk), jnp.float32))
        dqt_ref[:, pl.ds(r0, blk)] = (dqt * scale).astype(dqt_ref.dtype)
        return carry

    lax.fori_loop(0, tokens_all // blk, query_block, 0)
    dk_ref[...] = (dk_acc[...] * scale).astype(dk_ref.dtype)
    dv_ref[...] = dv_acc[...].astype(dv_ref.dtype)


def item_gradients(queries, key_vectors, value_vectors, out_grad):
    tokens_all, head_width = queries.shape
    out = jax.ShapeDtypeStruct((tokens_all, head_width), jnp.bfloat16)
    out_t = jax.ShapeDtypeStruct((head_width, tokens_all), jnp.bfloat16)
    dqt, dk, dv = pl.pallas_call(
        _kernel,
        out_shape=(out_t, out, out),
        scratch_shapes=[
            pltpu.VMEM((tokens_all, BLOCK), jnp.float32),
            pltpu.VMEM((tokens_all, BLOCK), jnp.float32),
            pltpu.VMEM((tokens_all, head_width), jnp.float32),
            pltpu.VMEM((tokens_all, head_width), jnp.float32),
        ],
        compiler_params=pltpu.CompilerParams(vmem_limit_bytes=32 * 1024 * 1024),
    )(queries, key_vectors, key_vectors.T, value_vectors, out_grad)
    return dqt.T, dk, dv


def body(queries, key_vectors, value_vectors, out_grad):
    page_count, tok_rows, feature_width = queries.shape
    seq_size = lax.psum(1, "seq")
    head_width = feature_width // HEADS
    per_dev = HEADS // seq_size
    tokens_all = seq_size * tok_rows
    inputs = (queries, key_vectors, value_vectors, out_grad)
    outs = []
    for page in range(page_count):
        part = jnp.stack(
            [x[page].reshape(tok_rows, seq_size, per_dev, head_width) for x in inputs]
        ).transpose(2, 0, 1, 3, 4)
        arrived = lax.all_to_all(part, "seq", split_axis=0, concat_axis=0, tiled=True)
        arrived = arrived.reshape(seq_size, 4, tok_rows, per_dev, head_width)
        grads = []
        for head in range(per_dev):
            items = [
                arrived[:, a, :, head, :].reshape(tokens_all, head_width) for a in range(4)
            ]
            grads.append(jnp.stack(item_gradients(*items)))
        grads = jnp.stack(grads).reshape(per_dev, 3, seq_size, tok_rows, head_width)
        grads = grads.transpose(2, 1, 0, 3, 4)
        returned = lax.all_to_all(grads, "seq", split_axis=0, concat_axis=0, tiled=True)
        outs.append(returned.transpose(1, 3, 0, 2, 4).reshape(3, tok_rows, feature_width))
    result = jnp.stack(outs, axis=1)
    return result[0], result[1], result[2]


def solution(mesh):
    placed = P("group", "seq", None)
    return jax.shard_map(
        body,
        mesh=mesh,
        in_specs=(placed, placed, placed, placed),
        out_specs=(placed, placed, placed),
        check_vma=False,
    )
```

```python
import functools

import jax
import jax.numpy as jnp
from jax import lax
from jax.experimental import pallas as pl
from jax.experimental.pallas import tpu as pltpu
from jax.sharding import PartitionSpec as P

HEADS = 32
BLOCK = 256


def _kernel(q_ref, k_ref, kt_ref, v_ref, do_ref, dqt_ref, dk_ref, dv_ref, s_scr, dp_scr, dk_acc, dv_acc):
    tokens_all, head_width = q_ref.shape
    blk = BLOCK
    scale = head_width ** (-0.5)
    dk_acc[...] = jnp.zeros_like(dk_acc)
    dv_acc[...] = jnp.zeros_like(dv_acc)
    contract_cols = (((1,), (1,)), ((), ()))
    key_ids = lax.broadcasted_iota(jnp.int32, (blk, blk), 0)
    query_ids = lax.broadcasted_iota(jnp.int32, (blk, blk), 1)

    def query_block(i, carry):
        r0 = pl.multiple_of(i * blk, blk)
        q = q_ref[pl.ds(r0, blk), :]
        do = do_ref[pl.ds(r0, blk), :]

        def scores(j, masked):
            c0 = pl.multiple_of(j * blk, blk)
            s = lax.dot_general(k_ref[pl.ds(c0, blk), :], q, contract_cols,
                                preferred_element_type=jnp.float32) * scale
            if masked:
                s = jnp.where(query_ids >= key_ids, s, -jnp.inf)
            s_scr[pl.ds(c0, blk), :] = s
            return jnp.max(s, axis=0, keepdims=True)

        top = lax.fori_loop(
            0, i, lambda j, t: jnp.maximum(t, scores(j, False)),
            jnp.full((1, blk), -jnp.inf, jnp.float32))
        top = jnp.maximum(top, scores(i, True))

        def weights_pass(j, sums):
            total, weighted = sums
            c0 = pl.multiple_of(j * blk, blk)
            w = jnp.exp(s_scr[pl.ds(c0, blk), :] - top)
            dp = lax.dot_general(v_ref[pl.ds(c0, blk), :], do, contract_cols,
                                 preferred_element_type=jnp.float32)
            s_scr[pl.ds(c0, blk), :] = w
            dp_scr[pl.ds(c0, blk), :] = dp
            return (total + jnp.sum(w, axis=0, keepdims=True),
                    weighted + jnp.sum(w * dp, axis=0, keepdims=True))

        zero_row = jnp.zeros((1, blk), jnp.float32)
        total, weighted = lax.fori_loop(0, i + 1, weights_pass, (zero_row, zero_row))
        inv_total = 1.0 / total
        delta = weighted * inv_total

        def grads_pass(j, dqt):
            c0 = pl.multiple_of(j * blk, blk)
            p = s_scr[pl.ds(c0, blk), :] * inv_total
            ds = (p * (dp_scr[pl.ds(c0, blk), :] - delta)).astype(jnp.bfloat16)
            dqt = dqt + jnp.dot(kt_ref[:, pl.ds(c0, blk)], ds, preferred_element_type=jnp.float32)
            dk_acc[pl.ds(c0, blk), :] += jnp.dot(ds, q, preferred_element_type=jnp.float32)
            dv_acc[pl.ds(c0, blk), :] += jnp.dot(
                p.astype(jnp.bfloat16), do, preferred_element_type=jnp.float32)
            return dqt

        dqt = lax.fori_loop(0, i + 1, grads_pass, jnp.zeros((head_width, blk), jnp.float32))
        dqt_ref[:, pl.ds(r0, blk)] = (dqt * scale).astype(dqt_ref.dtype)
        return carry

    lax.fori_loop(0, tokens_all // blk, query_block, 0)
    dk_ref[...] = (dk_acc[...] * scale).astype(dk_ref.dtype)
    dv_ref[...] = dv_acc[...].astype(dv_ref.dtype)


def item_gradients(queries, key_vectors, value_vectors, out_grad):
    tokens_all, head_width = queries.shape
    out = jax.ShapeDtypeStruct((tokens_all, head_width), jnp.bfloat16)
    out_t = jax.ShapeDtypeStruct((head_width, tokens_all), jnp.bfloat16)
    dqt, dk, dv = pl.pallas_call(
        _kernel,
        out_shape=(out_t, out, out),
        scratch_shapes=[
            pltpu.VMEM((tokens_all, BLOCK), jnp.float32),
            pltpu.VMEM((tokens_all, BLOCK), jnp.float32),
            pltpu.VMEM((tokens_all, head_width), jnp.float32),
            pltpu.VMEM((tokens_all, head_width), jnp.float32),
        ],
        compiler_params=pltpu.CompilerParams(vmem_limit_bytes=32 * 1024 * 1024),
    )(queries, key_vectors, key_vectors.T, value_vectors, out_grad)
    return dqt.T, dk, dv


def _gather_kernel(*refs, groups, per_dev, head_width):
    in_refs, out_ref = refs[:4], refs[4]
    for s in range(groups):
        for a, x_ref in enumerate(in_refs):
            for h in range(per_dev):
                col = (s * per_dev + h) * head_width
                out_ref[s, a, h] = x_ref[0, :, col:col + head_width]


def to_owners(inputs, page, seq_size, per_dev, head_width):
    page_count, tok_rows, feature_width = inputs[0].shape
    groups = max(1, 8 // per_dev)
    while seq_size % groups:
        groups //= 2
    width = groups * per_dev * head_width
    in_spec = pl.BlockSpec((1, tok_rows, width), lambda g: (page, 0, g))
    out_spec = pl.BlockSpec((groups, 4, per_dev, tok_rows, head_width), lambda g: (g, 0, 0, 0, 0))
    return pl.pallas_call(
        functools.partial(_gather_kernel, groups=groups, per_dev=per_dev, head_width=head_width),
        grid=(seq_size // groups,),
        in_specs=[in_spec] * 4,
        out_specs=out_spec,
        out_shape=jax.ShapeDtypeStruct((seq_size, 4, per_dev, tok_rows, head_width), inputs[0].dtype),
    )(*inputs)


def _scatter_kernel(ret_ref, a_in, b_in, c_in, a_out, b_out, c_out, *, groups, per_dev, head_width):
    del a_in, b_in, c_in
    for s in range(groups):
        for a, o_ref in enumerate((a_out, b_out, c_out)):
            for h in range(per_dev):
                col = (s * per_dev + h) * head_width
                o_ref[0, :, col:col + head_width] = ret_ref[s, a, h]


def from_owners(returned, results, page, per_dev, head_width):
    seq_size = returned.shape[0]
    page_count, tok_rows, feature_width = results[0].shape
    groups = max(1, 8 // per_dev)
    while seq_size % groups:
        groups //= 2
    width = groups * per_dev * head_width
    in_spec = pl.BlockSpec((groups, 3, per_dev, tok_rows, head_width), lambda g: (g, 0, 0, 0, 0))
    res_spec = pl.BlockSpec((1, tok_rows, width), lambda g: (page, 0, g))
    shape = jax.ShapeDtypeStruct(results[0].shape, results[0].dtype)
    return pl.pallas_call(
        functools.partial(_scatter_kernel, groups=groups, per_dev=per_dev, head_width=head_width),
        grid=(seq_size // groups,),
        in_specs=[in_spec, pl.BlockSpec(memory_space=pl.ANY)] + [pl.BlockSpec(memory_space=pl.ANY)] * 2,
        out_specs=[res_spec] * 3,
        out_shape=[shape] * 3,
        input_output_aliases={1: 0, 2: 1, 3: 2},
    )(returned, *results)


def body(queries, key_vectors, value_vectors, out_grad):
    page_count, tok_rows, feature_width = queries.shape
    seq_size = lax.psum(1, "seq")
    head_width = feature_width // HEADS
    per_dev = HEADS // seq_size
    tokens_all = seq_size * tok_rows
    inputs = (queries, key_vectors, value_vectors, out_grad)
    results = tuple(jnp.zeros_like(queries) for _ in range(3))
    for page in range(page_count):
        part = to_owners(inputs, page, seq_size, per_dev, head_width)
        arrived = lax.all_to_all(part, "seq", split_axis=0, concat_axis=0, tiled=True)
        grads = []
        for head in range(per_dev):
            items = [arrived[:, a, head].reshape(tokens_all, head_width) for a in range(4)]
            grads.append(jnp.stack(item_gradients(*items)))
        grads = jnp.stack(grads).reshape(per_dev, 3, seq_size, tok_rows, head_width)
        grads = grads.transpose(2, 1, 0, 3, 4)
        returned = lax.all_to_all(grads, "seq", split_axis=0, concat_axis=0, tiled=True)
        results = tuple(from_owners(returned, results, page, per_dev, head_width))
    return results


def solution(mesh):
    placed = P("group", "seq", None)
    return jax.shard_map(
        body,
        mesh=mesh,
        in_specs=(placed, placed, placed, placed),
        out_specs=(placed, placed, placed),
        check_vma=False,
    )
```

```python
import functools

import jax
import jax.numpy as jnp
from jax import lax
from jax.experimental import pallas as pl
from jax.experimental.pallas import tpu as pltpu
from jax.sharding import PartitionSpec as P

HEADS = 32
BLOCK = 512


def _kernel(q_ref, k_ref, kt_ref, v_ref, do_ref, dqt_ref, dk_ref, dv_ref, s_scr, dp_scr, dk_acc, dv_acc):
    tokens_all, head_width = q_ref.shape
    blk = BLOCK
    scale = head_width ** (-0.5)
    dk_acc[...] = jnp.zeros_like(dk_acc)
    dv_acc[...] = jnp.zeros_like(dv_acc)
    contract_cols = (((1,), (1,)), ((), ()))
    key_ids = lax.broadcasted_iota(jnp.int32, (blk, blk), 0)
    query_ids = lax.broadcasted_iota(jnp.int32, (blk, blk), 1)

    def query_block(i, carry):
        r0 = pl.multiple_of(i * blk, blk)
        q = q_ref[pl.ds(r0, blk), :]
        do = do_ref[pl.ds(r0, blk), :]

        def scores(j, masked):
            c0 = pl.multiple_of(j * blk, blk)
            s = lax.dot_general(k_ref[pl.ds(c0, blk), :], q, contract_cols,
                                preferred_element_type=jnp.float32) * scale
            if masked:
                s = jnp.where(query_ids >= key_ids, s, -jnp.inf)
            s_scr[pl.ds(c0, blk), :] = s
            return jnp.max(s, axis=0, keepdims=True)

        top = lax.fori_loop(
            0, i, lambda j, t: jnp.maximum(t, scores(j, False)),
            jnp.full((1, blk), -jnp.inf, jnp.float32))
        top = jnp.maximum(top, scores(i, True))

        def weights_pass(j, sums):
            total, weighted = sums
            c0 = pl.multiple_of(j * blk, blk)
            w = jnp.exp(s_scr[pl.ds(c0, blk), :] - top)
            dp = lax.dot_general(v_ref[pl.ds(c0, blk), :], do, contract_cols,
                                 preferred_element_type=jnp.float32)
            s_scr[pl.ds(c0, blk), :] = w
            dp_scr[pl.ds(c0, blk), :] = dp
            return (total + jnp.sum(w, axis=0, keepdims=True),
                    weighted + jnp.sum(w * dp, axis=0, keepdims=True))

        zero_row = jnp.zeros((1, blk), jnp.float32)
        total, weighted = lax.fori_loop(0, i + 1, weights_pass, (zero_row, zero_row))
        inv_total = 1.0 / total
        delta = weighted * inv_total

        def grads_pass(j, dqt):
            c0 = pl.multiple_of(j * blk, blk)
            p = s_scr[pl.ds(c0, blk), :] * inv_total
            ds = (p * (dp_scr[pl.ds(c0, blk), :] - delta)).astype(jnp.bfloat16)
            dqt = dqt + jnp.dot(kt_ref[:, pl.ds(c0, blk)], ds, preferred_element_type=jnp.float32)
            dk_acc[pl.ds(c0, blk), :] += jnp.dot(ds, q, preferred_element_type=jnp.float32)
            dv_acc[pl.ds(c0, blk), :] += jnp.dot(
                p.astype(jnp.bfloat16), do, preferred_element_type=jnp.float32)
            return dqt

        dqt = lax.fori_loop(0, i + 1, grads_pass, jnp.zeros((head_width, blk), jnp.float32))
        dqt_ref[:, pl.ds(r0, blk)] = (dqt * scale).astype(dqt_ref.dtype)
        return carry

    lax.fori_loop(0, tokens_all // blk, query_block, 0)
    dk_ref[...] = (dk_acc[...] * scale).astype(dk_ref.dtype)
    dv_ref[...] = dv_acc[...].astype(dv_ref.dtype)


def item_gradients(queries, key_vectors, value_vectors, out_grad):
    tokens_all, head_width = queries.shape
    out = jax.ShapeDtypeStruct((tokens_all, head_width), jnp.bfloat16)
    out_t = jax.ShapeDtypeStruct((head_width, tokens_all), jnp.bfloat16)
    dqt, dk, dv = pl.pallas_call(
        _kernel,
        out_shape=(out_t, out, out),
        scratch_shapes=[
            pltpu.VMEM((tokens_all, BLOCK), jnp.float32),
            pltpu.VMEM((tokens_all, BLOCK), jnp.float32),
            pltpu.VMEM((tokens_all, head_width), jnp.float32),
            pltpu.VMEM((tokens_all, head_width), jnp.float32),
        ],
        compiler_params=pltpu.CompilerParams(vmem_limit_bytes=32 * 1024 * 1024),
    )(queries, key_vectors, key_vectors.T, value_vectors, out_grad)
    return dqt.T, dk, dv


def _gather_kernel(*refs, groups, per_dev, head_width):
    in_refs, out_ref = refs[:4], refs[4]
    for s in range(groups):
        for a, x_ref in enumerate(in_refs):
            for h in range(per_dev):
                col = (s * per_dev + h) * head_width
                out_ref[s, a, h] = x_ref[0, :, col:col + head_width]


def to_owners(inputs, page, seq_size, per_dev, head_width):
    page_count, tok_rows, feature_width = inputs[0].shape
    groups = max(1, 8 // per_dev)
    while seq_size % groups:
        groups //= 2
    width = groups * per_dev * head_width
    in_spec = pl.BlockSpec((1, tok_rows, width), lambda g: (page, 0, g))
    out_spec = pl.BlockSpec((groups, 4, per_dev, tok_rows, head_width), lambda g: (g, 0, 0, 0, 0))
    return pl.pallas_call(
        functools.partial(_gather_kernel, groups=groups, per_dev=per_dev, head_width=head_width),
        grid=(seq_size // groups,),
        in_specs=[in_spec] * 4,
        out_specs=out_spec,
        out_shape=jax.ShapeDtypeStruct((seq_size, 4, per_dev, tok_rows, head_width), inputs[0].dtype),
    )(*inputs)


def _scatter_kernel(ret_ref, a_in, b_in, c_in, a_out, b_out, c_out, *, groups, per_dev, head_width):
    del a_in, b_in, c_in
    for s in range(groups):
        for a, o_ref in enumerate((a_out, b_out, c_out)):
            for h in range(per_dev):
                col = (s * per_dev + h) * head_width
                o_ref[0, :, col:col + head_width] = ret_ref[s, a, h]


def from_owners(returned, results, page, per_dev, head_width):
    seq_size = returned.shape[0]
    page_count, tok_rows, feature_width = results[0].shape
    groups = max(1, 8 // per_dev)
    while seq_size % groups:
        groups //= 2
    width = groups * per_dev * head_width
    in_spec = pl.BlockSpec((groups, 3, per_dev, tok_rows, head_width), lambda g: (g, 0, 0, 0, 0))
    res_spec = pl.BlockSpec((1, tok_rows, width), lambda g: (page, 0, g))
    shape = jax.ShapeDtypeStruct(results[0].shape, results[0].dtype)
    return pl.pallas_call(
        functools.partial(_scatter_kernel, groups=groups, per_dev=per_dev, head_width=head_width),
        grid=(seq_size // groups,),
        in_specs=[in_spec, pl.BlockSpec(memory_space=pl.ANY)] + [pl.BlockSpec(memory_space=pl.ANY)] * 2,
        out_specs=[res_spec] * 3,
        out_shape=[shape] * 3,
        input_output_aliases={1: 0, 2: 1, 3: 2},
    )(returned, *results)


def body(queries, key_vectors, value_vectors, out_grad):
    page_count, tok_rows, feature_width = queries.shape
    seq_size = lax.psum(1, "seq")
    head_width = feature_width // HEADS
    per_dev = HEADS // seq_size
    tokens_all = seq_size * tok_rows
    inputs = (queries, key_vectors, value_vectors, out_grad)
    results = tuple(jnp.zeros_like(queries) for _ in range(3))
    for page in range(page_count):
        part = to_owners(inputs, page, seq_size, per_dev, head_width)
        arrived = lax.all_to_all(part, "seq", split_axis=0, concat_axis=0, tiled=True)
        grads = []
        for head in range(per_dev):
            items = [arrived[:, a, head].reshape(tokens_all, head_width) for a in range(4)]
            grads.append(jnp.stack(item_gradients(*items)))
        grads = jnp.stack(grads).reshape(per_dev, 3, seq_size, tok_rows, head_width)
        grads = grads.transpose(2, 1, 0, 3, 4)
        returned = lax.all_to_all(grads, "seq", split_axis=0, concat_axis=0, tiled=True)
        results = tuple(from_owners(returned, results, page, per_dev, head_width))
    return results


def solution(mesh):
    placed = P("group", "seq", None)
    return jax.shard_map(
        body,
        mesh=mesh,
        in_specs=(placed, placed, placed, placed),
        out_specs=(placed, placed, placed),
        check_vma=False,
    )
```

```python
import functools

import jax
import jax.numpy as jnp
from jax import lax
from jax.experimental import pallas as pl
from jax.experimental.pallas import tpu as pltpu
from jax.sharding import PartitionSpec as P


HEADS = 32
BLOCK = 512


def _kernel(q_ref, k_ref, kt_ref, v_ref, do_ref, dqt_ref, dk_ref, dv_ref, s_scr, dp_scr, dk_acc, dv_acc):
    tokens_all, head_width = q_ref.shape
    blk = BLOCK
    scale = head_width ** (-0.5)
    dk_acc[...] = jnp.zeros_like(dk_acc)
    dv_acc[...] = jnp.zeros_like(dv_acc)
    contract_cols = (((1,), (1,)), ((), ()))
    key_ids = lax.broadcasted_iota(jnp.int32, (blk, blk), 0)
    query_ids = lax.broadcasted_iota(jnp.int32, (blk, blk), 1)

    def query_block(i, carry):
        r0 = pl.multiple_of(i * blk, blk)
        q = q_ref[pl.ds(r0, blk), :]
        do = do_ref[pl.ds(r0, blk), :]

        def scores(j, masked):
            c0 = pl.multiple_of(j * blk, blk)
            s = lax.dot_general(k_ref[pl.ds(c0, blk), :], q, contract_cols,
                                preferred_element_type=jnp.float32) * scale
            if masked:
                s = jnp.where(query_ids >= key_ids, s, -jnp.inf)
            s_scr[pl.ds(c0, blk), :] = s
            return jnp.max(s, axis=0, keepdims=True)

        top = lax.fori_loop(
            0, i, lambda j, t: jnp.maximum(t, scores(j, False)),
            jnp.full((1, blk), -jnp.inf, jnp.float32))
        top = jnp.maximum(top, scores(i, True))

        def weights_pass(j, sums):
            total, weighted = sums
            c0 = pl.multiple_of(j * blk, blk)
            w = jnp.exp(s_scr[pl.ds(c0, blk), :] - top)
            dp = lax.dot_general(v_ref[pl.ds(c0, blk), :], do, contract_cols,
                                 preferred_element_type=jnp.float32)
            s_scr[pl.ds(c0, blk), :] = w
            dp_scr[pl.ds(c0, blk), :] = dp
            return (total + jnp.sum(w, axis=0, keepdims=True),
                    weighted + jnp.sum(w * dp, axis=0, keepdims=True))

        zero_row = jnp.zeros((1, blk), jnp.float32)
        total, weighted = lax.fori_loop(0, i + 1, weights_pass, (zero_row, zero_row))
        inv_total = 1.0 / total
        delta = weighted * inv_total

        def grads_pass(j, dqt):
            c0 = pl.multiple_of(j * blk, blk)
            p = s_scr[pl.ds(c0, blk), :] * inv_total
            ds = (p * (dp_scr[pl.ds(c0, blk), :] - delta)).astype(jnp.bfloat16)
            dqt = dqt + jnp.dot(kt_ref[:, pl.ds(c0, blk)], ds, preferred_element_type=jnp.float32)
            dk_acc[pl.ds(c0, blk), :] += jnp.dot(ds, q, preferred_element_type=jnp.float32)
            dv_acc[pl.ds(c0, blk), :] += jnp.dot(
                p.astype(jnp.bfloat16), do, preferred_element_type=jnp.float32)
            return dqt

        dqt = lax.fori_loop(0, i + 1, grads_pass, jnp.zeros((head_width, blk), jnp.float32))
        dqt_ref[:, pl.ds(r0, blk)] = (dqt * scale).astype(dqt_ref.dtype)
        return carry

    lax.fori_loop(0, tokens_all // blk, query_block, 0)
    dk_ref[...] = (dk_acc[...] * scale).astype(dk_ref.dtype)
    dv_ref[...] = dv_acc[...].astype(dv_ref.dtype)


def item_gradients(queries, key_vectors, value_vectors, out_grad):
    tokens_all, head_width = queries.shape
    out = jax.ShapeDtypeStruct((tokens_all, head_width), jnp.bfloat16)
    out_t = jax.ShapeDtypeStruct((head_width, tokens_all), jnp.bfloat16)
    dqt, dk, dv = pl.pallas_call(
        _kernel,
        out_shape=(out_t, out, out),
        scratch_shapes=[
            pltpu.VMEM((tokens_all, BLOCK), jnp.float32),
            pltpu.VMEM((tokens_all, BLOCK), jnp.float32),
            pltpu.VMEM((tokens_all, head_width), jnp.float32),
            pltpu.VMEM((tokens_all, head_width), jnp.float32),
        ],
        compiler_params=pltpu.CompilerParams(vmem_limit_bytes=32 * 1024 * 1024),
    )(queries, key_vectors, key_vectors.T, value_vectors, out_grad)
    return dqt.T, dk, dv


def _gather_kernel(*refs, groups, per_dev, head_width):
    in_refs, out_ref = refs[:4], refs[4]
    for s in range(groups):
        for a, x_ref in enumerate(in_refs):
            for h in range(per_dev):
                col = (s * per_dev + h) * head_width
                out_ref[s, a, h] = x_ref[0, :, col:col + head_width]


def to_owners(inputs, page, seq_size, per_dev, head_width):
    _, tok_rows, _ = inputs[0].shape
    groups = max(1, 8 // per_dev)
    while seq_size % groups:
        groups //= 2
    width = groups * per_dev * head_width
    in_spec = pl.BlockSpec((1, tok_rows, width), lambda g: (page, 0, g))
    out_spec = pl.BlockSpec((groups, 4, per_dev, tok_rows, head_width), lambda g: (g, 0, 0, 0, 0))
    return pl.pallas_call(
        functools.partial(_gather_kernel, groups=groups, per_dev=per_dev, head_width=head_width),
        grid=(seq_size // groups,),
        in_specs=[in_spec] * 4,
        out_specs=out_spec,
        out_shape=jax.ShapeDtypeStruct((seq_size, 4, per_dev, tok_rows, head_width), inputs[0].dtype),
    )(*inputs)


def _scatter_kernel(ret_ref, a_in, b_in, c_in, a_out, b_out, c_out, *, groups, per_dev, head_width):
    del a_in, b_in, c_in
    for s in range(groups):
        for a, o_ref in enumerate((a_out, b_out, c_out)):
            for h in range(per_dev):
                col = (s * per_dev + h) * head_width
                o_ref[0, :, col:col + head_width] = ret_ref[s, a, h]


def from_owners(returned, results, page, per_dev, head_width):
    seq_size = returned.shape[0]
    _, tok_rows, _ = results[0].shape
    groups = max(1, 8 // per_dev)
    while seq_size % groups:
        groups //= 2
    width = groups * per_dev * head_width
    in_spec = pl.BlockSpec((groups, 3, per_dev, tok_rows, head_width), lambda g: (g, 0, 0, 0, 0))
    res_spec = pl.BlockSpec((1, tok_rows, width), lambda g: (page, 0, g))
    shape = jax.ShapeDtypeStruct(results[0].shape, results[0].dtype)
    return pl.pallas_call(
        functools.partial(_scatter_kernel, groups=groups, per_dev=per_dev, head_width=head_width),
        grid=(seq_size // groups,),
        in_specs=[in_spec, pl.BlockSpec(memory_space=pl.ANY)] + [pl.BlockSpec(memory_space=pl.ANY)] * 2,
        out_specs=[res_spec] * 3,
        out_shape=[shape] * 3,
        input_output_aliases={1: 0, 2: 1, 3: 2},
    )(returned, *results)


def exchange(x, seq_size):
    me = lax.axis_index("seq")
    out = x
    for shift in range(1, seq_size):
        piece = lax.dynamic_index_in_dim(x, (me + shift) % seq_size, 0)
        perm = [(i, (i + shift) % seq_size) for i in range(seq_size)]
        got = lax.ppermute(piece, "seq", perm)
        out = lax.dynamic_update_index_in_dim(out, got[0], (me - shift) % seq_size, 0)
    return out


def body(queries, key_vectors, value_vectors, out_grad):
    page_count, tok_rows, feature_width = queries.shape
    seq_size = lax.psum(1, "seq")
    head_width = feature_width // HEADS
    per_dev = HEADS // seq_size
    tokens_all = seq_size * tok_rows
    inputs = (queries, key_vectors, value_vectors, out_grad)
    results = tuple(jnp.zeros_like(queries) for _ in range(3))
    for page in range(page_count):
        part = to_owners(inputs, page, seq_size, per_dev, head_width)
        arrived = exchange(part, seq_size)
        grads = []
        for head in range(per_dev):
            items = [arrived[:, a, head].reshape(tokens_all, head_width) for a in range(4)]
            grads.append(jnp.stack(item_gradients(*items)))
        grads = jnp.stack(grads).reshape(per_dev, 3, seq_size, tok_rows, head_width)
        grads = grads.transpose(2, 1, 0, 3, 4)
        returned = exchange(grads, seq_size)
        results = tuple(from_owners(returned, results, page, per_dev, head_width))
    return results


def solution(mesh):
    placed = P("group", "seq", None)
    return jax.shard_map(
        body,
        mesh=mesh,
        in_specs=(placed, placed, placed, placed),
        out_specs=(placed, placed, placed),
        check_vma=False,
    )
```

```python
import functools

import jax
import jax.numpy as jnp
from jax import lax
from jax.experimental import pallas as pl
from jax.experimental.pallas import tpu as pltpu
from jax.sharding import PartitionSpec as P

HEADS = 32
BLOCK = 512


def _kernel(q_ref, k_ref, kt_ref, v_ref, do_ref, dqt_ref, dk_ref, dv_ref, s_scr, dp_scr, dk_acc, dv_acc):
    tokens_all, head_width = q_ref.shape
    blk = BLOCK
    scale = head_width ** (-0.5)
    dk_acc[...] = jnp.zeros_like(dk_acc)
    dv_acc[...] = jnp.zeros_like(dv_acc)
    contract_cols = (((1,), (1,)), ((), ()))
    key_ids = lax.broadcasted_iota(jnp.int32, (blk, blk), 0)
    query_ids = lax.broadcasted_iota(jnp.int32, (blk, blk), 1)

    def query_block(i, carry):
        r0 = pl.multiple_of(i * blk, blk)
        q = q_ref[pl.ds(r0, blk), :]
        do = do_ref[pl.ds(r0, blk), :]

        def scores(j, masked):
            c0 = pl.multiple_of(j * blk, blk)
            s = lax.dot_general(k_ref[pl.ds(c0, blk), :], q, contract_cols,
                                preferred_element_type=jnp.float32) * scale
            if masked:
                s = jnp.where(query_ids >= key_ids, s, -jnp.inf)
            s_scr[pl.ds(c0, blk), :] = s
            return jnp.max(s, axis=0, keepdims=True)

        top = lax.fori_loop(
            0, i, lambda j, t: jnp.maximum(t, scores(j, False)),
            jnp.full((1, blk), -jnp.inf, jnp.float32))
        top = jnp.maximum(top, scores(i, True))

        def weights_pass(j, sums):
            total, weighted = sums
            c0 = pl.multiple_of(j * blk, blk)
            w = jnp.exp(s_scr[pl.ds(c0, blk), :] - top)
            dp = lax.dot_general(v_ref[pl.ds(c0, blk), :], do, contract_cols,
                                 preferred_element_type=jnp.float32)
            s_scr[pl.ds(c0, blk), :] = w
            dp_scr[pl.ds(c0, blk), :] = dp
            return (total + jnp.sum(w, axis=0, keepdims=True),
                    weighted + jnp.sum(w * dp, axis=0, keepdims=True))

        zero_row = jnp.zeros((1, blk), jnp.float32)
        total, weighted = lax.fori_loop(0, i + 1, weights_pass, (zero_row, zero_row))
        inv_total = 1.0 / total
        delta = weighted * inv_total

        def grads_pass(j, dqt):
            c0 = pl.multiple_of(j * blk, blk)
            p = s_scr[pl.ds(c0, blk), :] * inv_total
            ds = (p * (dp_scr[pl.ds(c0, blk), :] - delta)).astype(jnp.bfloat16)
            dqt = dqt + jnp.dot(kt_ref[:, pl.ds(c0, blk)], ds, preferred_element_type=jnp.float32)
            dk_acc[pl.ds(c0, blk), :] += jnp.dot(ds, q, preferred_element_type=jnp.float32)
            dv_acc[pl.ds(c0, blk), :] += jnp.dot(
                p.astype(jnp.bfloat16), do, preferred_element_type=jnp.float32)
            return dqt

        dqt = lax.fori_loop(0, i + 1, grads_pass, jnp.zeros((head_width, blk), jnp.float32))
        dqt_ref[:, pl.ds(r0, blk)] = (dqt * scale).astype(dqt_ref.dtype)
        return carry

    lax.fori_loop(0, tokens_all // blk, query_block, 0)
    dk_ref[...] = (dk_acc[...] * scale).astype(dk_ref.dtype)
    dv_ref[...] = dv_acc[...].astype(dv_ref.dtype)


def item_gradients(queries, key_vectors, value_vectors, out_grad):
    tokens_all, head_width = queries.shape
    out = jax.ShapeDtypeStruct((tokens_all, head_width), jnp.bfloat16)
    out_t = jax.ShapeDtypeStruct((head_width, tokens_all), jnp.bfloat16)
    dqt, dk, dv = pl.pallas_call(
        _kernel,
        out_shape=(out_t, out, out),
        scratch_shapes=[
            pltpu.VMEM((tokens_all, BLOCK), jnp.float32),
            pltpu.VMEM((tokens_all, BLOCK), jnp.float32),
            pltpu.VMEM((tokens_all, head_width), jnp.float32),
            pltpu.VMEM((tokens_all, head_width), jnp.float32),
        ],
        compiler_params=pltpu.CompilerParams(vmem_limit_bytes=32 * 1024 * 1024),
    )(queries, key_vectors, key_vectors.T, value_vectors, out_grad)
    return dqt.T, dk, dv


def _gather_kernel(*refs, groups, per_dev, head_width):
    in_refs, out_ref = refs[:4], refs[4]
    for s in range(groups):
        for a, x_ref in enumerate(in_refs):
            for h in range(per_dev):
                col = (s * per_dev + h) * head_width
                out_ref[s, a, h] = x_ref[0, :, col:col + head_width]


def to_owners(inputs, page, seq_size, per_dev, head_width):
    page_count, tok_rows, feature_width = inputs[0].shape
    groups = max(1, seq_size // 2)
    while seq_size % groups:
        groups //= 2
    width = groups * per_dev * head_width
    in_spec = pl.BlockSpec((1, tok_rows, width), lambda g: (page, 0, g))
    out_spec = pl.BlockSpec((groups, 4, per_dev, tok_rows, head_width), lambda g: (g, 0, 0, 0, 0))
    return pl.pallas_call(
        functools.partial(_gather_kernel, groups=groups, per_dev=per_dev, head_width=head_width),
        grid=(seq_size // groups,),
        in_specs=[in_spec] * 4,
        out_specs=out_spec,
        out_shape=jax.ShapeDtypeStruct((seq_size, 4, per_dev, tok_rows, head_width), inputs[0].dtype),
    )(*inputs)


def _scatter_kernel(ret_ref, a_in, b_in, c_in, a_out, b_out, c_out, *, groups, per_dev, head_width):
    del a_in, b_in, c_in
    for s in range(groups):
        for a, o_ref in enumerate((a_out, b_out, c_out)):
            for h in range(per_dev):
                col = (s * per_dev + h) * head_width
                o_ref[0, :, col:col + head_width] = ret_ref[s, a, h]


def from_owners(returned, results, page, per_dev, head_width):
    seq_size = returned.shape[0]
    page_count, tok_rows, feature_width = results[0].shape
    groups = max(1, seq_size // 2)
    while seq_size % groups:
        groups //= 2
    width = groups * per_dev * head_width
    in_spec = pl.BlockSpec((groups, 3, per_dev, tok_rows, head_width), lambda g: (g, 0, 0, 0, 0))
    res_spec = pl.BlockSpec((1, tok_rows, width), lambda g: (page, 0, g))
    shape = jax.ShapeDtypeStruct(results[0].shape, results[0].dtype)
    return pl.pallas_call(
        functools.partial(_scatter_kernel, groups=groups, per_dev=per_dev, head_width=head_width),
        grid=(seq_size // groups,),
        in_specs=[in_spec, pl.BlockSpec(memory_space=pl.ANY)] + [pl.BlockSpec(memory_space=pl.ANY)] * 2,
        out_specs=[res_spec] * 3,
        out_shape=[shape] * 3,
        input_output_aliases={1: 0, 2: 1, 3: 2},
    )(returned, *results)


def body(queries, key_vectors, value_vectors, out_grad):
    page_count, tok_rows, feature_width = queries.shape
    seq_size = lax.psum(1, "seq")
    head_width = feature_width // HEADS
    per_dev = HEADS // seq_size
    tokens_all = seq_size * tok_rows
    inputs = (queries, key_vectors, value_vectors, out_grad)
    results = tuple(jnp.zeros_like(queries) for _ in range(3))
    for page in range(page_count):
        part = to_owners(inputs, page, seq_size, per_dev, head_width)
        arrived = lax.all_to_all(part, "seq", split_axis=0, concat_axis=0, tiled=True)
        grads = []
        for head in range(per_dev):
            items = [arrived[:, a, head].reshape(tokens_all, head_width) for a in range(4)]
            grads.append(jnp.stack(item_gradients(*items)))
        grads = jnp.stack(grads).reshape(per_dev, 3, seq_size, tok_rows, head_width)
        grads = grads.transpose(2, 1, 0, 3, 4)
        returned = lax.all_to_all(grads, "seq", split_axis=0, concat_axis=0, tiled=True)
        results = tuple(from_owners(returned, results, page, per_dev, head_width))
    return results


def solution(mesh):
    placed = P("group", "seq", None)
    return jax.shard_map(
        body,
        mesh=mesh,
        in_specs=(placed, placed, placed, placed),
        out_specs=(placed, placed, placed),
        check_vma=False,
    )
```

```python
import functools

import jax
import jax.numpy as jnp
from jax import lax
from jax.experimental import pallas as pl
from jax.experimental.pallas import tpu as pltpu
from jax.sharding import PartitionSpec as P

HEADS = 32
BLOCK = 512


def _kernel(q_ref, k_ref, v_ref, do_ref, dq_ref, dk_ref, dv_ref, s_scr, dp_scr, dk_acc, dv_acc, kt_scr):
    owners, tok_rows, head_width = q_ref.shape
    tokens_all = owners * tok_rows
    blk = BLOCK
    per_blk = blk // tok_rows
    scale = head_width ** (-0.5)
    dk_acc[...] = jnp.zeros_like(dk_acc)
    dv_acc[...] = jnp.zeros_like(dv_acc)
    contract_cols = (((1,), (1,)), ((), ()))
    key_ids = lax.broadcasted_iota(jnp.int32, (blk, blk), 0)
    query_ids = lax.broadcasted_iota(jnp.int32, (blk, blk), 1)

    def rows(ref, j):
        o0 = pl.multiple_of(j * per_blk, per_blk)
        return ref[pl.ds(o0, per_blk)].reshape(blk, head_width)

    def fill_kt(j, carry):
        c0 = pl.multiple_of(j * blk, blk)
        kt_scr[:, pl.ds(c0, blk)] = rows(k_ref, j).T
        return carry

    lax.fori_loop(0, tokens_all // blk, fill_kt, 0)

    def query_block(i, carry):
        q = rows(q_ref, i)
        do = rows(do_ref, i)

        def scores(j, masked):
            c0 = pl.multiple_of(j * blk, blk)
            s = lax.dot_general(rows(k_ref, j), q, contract_cols,
                                preferred_element_type=jnp.float32) * scale
            if masked:
                s = jnp.where(query_ids >= key_ids, s, -jnp.inf)
            s_scr[pl.ds(c0, blk), :] = s
            return jnp.max(s, axis=0, keepdims=True)

        top = lax.fori_loop(
            0, i, lambda j, t: jnp.maximum(t, scores(j, False)),
            jnp.full((1, blk), -jnp.inf, jnp.float32))
        top = jnp.maximum(top, scores(i, True))

        def weights_pass(j, sums):
            total, weighted = sums
            c0 = pl.multiple_of(j * blk, blk)
            w = jnp.exp(s_scr[pl.ds(c0, blk), :] - top)
            dp = lax.dot_general(rows(v_ref, j), do, contract_cols,
                                 preferred_element_type=jnp.float32)
            s_scr[pl.ds(c0, blk), :] = w
            dp_scr[pl.ds(c0, blk), :] = dp
            return (total + jnp.sum(w, axis=0, keepdims=True),
                    weighted + jnp.sum(w * dp, axis=0, keepdims=True))

        zero_row = jnp.zeros((1, blk), jnp.float32)
        total, weighted = lax.fori_loop(0, i + 1, weights_pass, (zero_row, zero_row))
        inv_total = 1.0 / total
        delta = weighted * inv_total

        def grads_pass(j, dqt):
            c0 = pl.multiple_of(j * blk, blk)
            p = s_scr[pl.ds(c0, blk), :] * inv_total
            ds = (p * (dp_scr[pl.ds(c0, blk), :] - delta)).astype(jnp.bfloat16)
            dqt = dqt + jnp.dot(kt_scr[:, pl.ds(c0, blk)], ds, preferred_element_type=jnp.float32)
            dk_acc[pl.ds(c0, blk), :] += jnp.dot(ds, q, preferred_element_type=jnp.float32)
            dv_acc[pl.ds(c0, blk), :] += jnp.dot(
                p.astype(jnp.bfloat16), do, preferred_element_type=jnp.float32)
            return dqt

        dqt = lax.fori_loop(0, i + 1, grads_pass, jnp.zeros((head_width, blk), jnp.float32))
        r0 = pl.multiple_of(i * blk, blk)
        dq_ref[pl.ds(r0, blk), :] = (dqt * scale).T.astype(dq_ref.dtype)
        return carry

    lax.fori_loop(0, tokens_all // blk, query_block, 0)
    dk_ref[...] = (dk_acc[...] * scale).astype(dk_ref.dtype)
    dv_ref[...] = dv_acc[...].astype(dv_ref.dtype)


def item_gradients(arrived, head):
    owners, _, _, tok_rows, head_width = arrived.shape
    tokens_all = owners * tok_rows
    out = jax.ShapeDtypeStruct((tokens_all, head_width), jnp.bfloat16)
    specs = [
        pl.BlockSpec((owners, None, None, tok_rows, head_width),
                     functools.partial(lambda a, i: (0, a, head, 0, 0), a))
        for a in range(4)
    ]
    return pl.pallas_call(
        _kernel,
        grid=(1,),
        in_specs=specs,
        out_specs=[pl.BlockSpec((tokens_all, head_width), lambda i: (0, 0))] * 3,
        out_shape=(out, out, out),
        scratch_shapes=[
            pltpu.VMEM((tokens_all, BLOCK), jnp.float32),
            pltpu.VMEM((tokens_all, BLOCK), jnp.float32),
            pltpu.VMEM((tokens_all, head_width), jnp.float32),
            pltpu.VMEM((tokens_all, head_width), jnp.float32),
            pltpu.VMEM((head_width, tokens_all), jnp.bfloat16),
        ],
        compiler_params=pltpu.CompilerParams(vmem_limit_bytes=40 * 1024 * 1024),
    )(arrived, arrived, arrived, arrived)


def _gather_kernel(*refs, groups, per_dev, head_width):
    in_refs, out_ref = refs[:4], refs[4]
    for s in range(groups):
        for a, x_ref in enumerate(in_refs):
            for h in range(per_dev):
                col = (s * per_dev + h) * head_width
                out_ref[s, a, h] = x_ref[0, :, col:col + head_width]


def to_owners(inputs, page, seq_size, per_dev, head_width):
    page_count, tok_rows, feature_width = inputs[0].shape
    groups = max(1, seq_size // 2)
    while seq_size % groups:
        groups //= 2
    width = groups * per_dev * head_width
    in_spec = pl.BlockSpec((1, tok_rows, width), lambda g: (page, 0, g))
    out_spec = pl.BlockSpec((groups, 4, per_dev, tok_rows, head_width), lambda g: (g, 0, 0, 0, 0))
    return pl.pallas_call(
        functools.partial(_gather_kernel, groups=groups, per_dev=per_dev, head_width=head_width),
        grid=(seq_size // groups,),
        in_specs=[in_spec] * 4,
        out_specs=out_spec,
        out_shape=jax.ShapeDtypeStruct((seq_size, 4, per_dev, tok_rows, head_width), inputs[0].dtype),
    )(*inputs)


def _scatter_kernel(ret_ref, a_in, b_in, c_in, a_out, b_out, c_out, *, groups, per_dev, head_width):
    del a_in, b_in, c_in
    for s in range(groups):
        for a, o_ref in enumerate((a_out, b_out, c_out)):
            for h in range(per_dev):
                col = (s * per_dev + h) * head_width
                o_ref[0, :, col:col + head_width] = ret_ref[s, a, h]


def from_owners(returned, results, page, per_dev, head_width):
    seq_size = returned.shape[0]
    page_count, tok_rows, feature_width = results[0].shape
    groups = max(1, seq_size // 2)
    while seq_size % groups:
        groups //= 2
    width = groups * per_dev * head_width
    in_spec = pl.BlockSpec((groups, 3, per_dev, tok_rows, head_width), lambda g: (g, 0, 0, 0, 0))
    res_spec = pl.BlockSpec((1, tok_rows, width), lambda g: (page, 0, g))
    shape = jax.ShapeDtypeStruct(results[0].shape, results[0].dtype)
    return pl.pallas_call(
        functools.partial(_scatter_kernel, groups=groups, per_dev=per_dev, head_width=head_width),
        grid=(seq_size // groups,),
        in_specs=[in_spec, pl.BlockSpec(memory_space=pl.ANY)] + [pl.BlockSpec(memory_space=pl.ANY)] * 2,
        out_specs=[res_spec] * 3,
        out_shape=[shape] * 3,
        input_output_aliases={1: 0, 2: 1, 3: 2},
    )(returned, *results)


def body(queries, key_vectors, value_vectors, out_grad):
    page_count, tok_rows, feature_width = queries.shape
    seq_size = lax.psum(1, "seq")
    head_width = feature_width // HEADS
    per_dev = HEADS // seq_size
    tokens_all = seq_size * tok_rows
    inputs = (queries, key_vectors, value_vectors, out_grad)
    results = tuple(jnp.zeros_like(queries) for _ in range(3))
    for page in range(page_count):
        part = to_owners(inputs, page, seq_size, per_dev, head_width)
        arrived = lax.all_to_all(part, "seq", split_axis=0, concat_axis=0, tiled=True)
        grads = []
        for head in range(per_dev):
            grads.append(jnp.stack(item_gradients(arrived, head)))
        grads = jnp.stack(grads).reshape(per_dev, 3, seq_size, tok_rows, head_width)
        grads = grads.transpose(2, 1, 0, 3, 4)
        returned = lax.all_to_all(grads, "seq", split_axis=0, concat_axis=0, tiled=True)
        results = tuple(from_owners(returned, results, page, per_dev, head_width))
    return results


def solution(mesh):
    placed = P("group", "seq", None)
    return jax.shard_map(
        body,
        mesh=mesh,
        in_specs=(placed, placed, placed, placed),
        out_specs=(placed, placed, placed),
        check_vma=False,
    )
```

```python
import functools

import jax
import jax.numpy as jnp
from jax import lax
from jax.experimental import pallas as pl
from jax.experimental.pallas import tpu as pltpu
from jax.sharding import PartitionSpec as P

HEADS = 32
BLOCK = 512


def _kernel(q_ref, k_ref, v_ref, do_ref, dq_ref, dk_ref, dv_ref, s_scr, dp_scr, dk_acc, dv_acc, kt_scr):
    owners, tok_rows, head_width = q_ref.shape
    tokens_all = owners * tok_rows
    blk = BLOCK
    per_blk = blk // tok_rows
    scale = head_width ** (-0.5)
    dk_acc[...] = jnp.zeros_like(dk_acc)
    dv_acc[...] = jnp.zeros_like(dv_acc)
    contract_cols = (((1,), (1,)), ((), ()))
    key_ids = lax.broadcasted_iota(jnp.int32, (blk, blk), 0)
    query_ids = lax.broadcasted_iota(jnp.int32, (blk, blk), 1)

    def rows(ref, j):
        o0 = pl.multiple_of(j * per_blk, per_blk)
        return ref[pl.ds(o0, per_blk)].reshape(blk, head_width)

    def fill_kt(j, carry):
        c0 = pl.multiple_of(j * blk, blk)
        kt_scr[:, pl.ds(c0, blk)] = rows(k_ref, j).T
        return carry

    lax.fori_loop(0, tokens_all // blk, fill_kt, 0)

    def query_block(i, carry):
        q = rows(q_ref, i)
        do = rows(do_ref, i)

        def scores(j, masked):
            c0 = pl.multiple_of(j * blk, blk)
            s = lax.dot_general(rows(k_ref, j), q, contract_cols,
                                preferred_element_type=jnp.float32) * scale
            if masked:
                s = jnp.where(query_ids >= key_ids, s, -jnp.inf)
            s_scr[pl.ds(c0, blk), :] = s
            return jnp.max(s, axis=0, keepdims=True)

        top = lax.fori_loop(
            0, i, lambda j, t: jnp.maximum(t, scores(j, False)),
            jnp.full((1, blk), -jnp.inf, jnp.float32))
        top = jnp.maximum(top, scores(i, True))

        def weights_pass(j, sums):
            total, weighted = sums
            c0 = pl.multiple_of(j * blk, blk)
            w = jnp.exp(s_scr[pl.ds(c0, blk), :] - top)
            dp = lax.dot_general(rows(v_ref, j), do, contract_cols,
                                 preferred_element_type=jnp.float32)
            s_scr[pl.ds(c0, blk), :] = w
            dp_scr[pl.ds(c0, blk), :] = dp
            return (total + jnp.sum(w, axis=0, keepdims=True),
                    weighted + jnp.sum(w * dp, axis=0, keepdims=True))

        zero_row = jnp.zeros((1, blk), jnp.float32)
        total, weighted = lax.fori_loop(0, i + 1, weights_pass, (zero_row, zero_row))
        inv_total = 1.0 / total
        delta = weighted * inv_total

        def grads_pass(j, dqt):
            c0 = pl.multiple_of(j * blk, blk)
            p = s_scr[pl.ds(c0, blk), :] * inv_total
            ds = (p * (dp_scr[pl.ds(c0, blk), :] - delta)).astype(jnp.bfloat16)
            dqt = dqt + jnp.dot(kt_scr[:, pl.ds(c0, blk)], ds, preferred_element_type=jnp.float32)
            dk_acc[pl.ds(c0, blk), :] += jnp.dot(ds, q, preferred_element_type=jnp.float32)
            dv_acc[pl.ds(c0, blk), :] += jnp.dot(
                p.astype(jnp.bfloat16), do, preferred_element_type=jnp.float32)
            return dqt

        dqt = lax.fori_loop(0, i + 1, grads_pass, jnp.zeros((head_width, blk), jnp.float32))
        r0 = pl.multiple_of(i * blk, blk)
        dq_ref[pl.ds(r0, blk), :] = (dqt * scale).T.astype(dq_ref.dtype)
        return carry

    lax.fori_loop(0, tokens_all // blk, query_block, 0)
    dk_ref[...] = (dk_acc[...] * scale).astype(dk_ref.dtype)
    dv_ref[...] = dv_acc[...].astype(dv_ref.dtype)


def item_gradients(arrived, head):
    owners, _, _, tok_rows, head_width = arrived.shape
    tokens_all = owners * tok_rows
    out = jax.ShapeDtypeStruct((tokens_all, head_width), jnp.bfloat16)
    specs = [
        pl.BlockSpec((owners, None, None, tok_rows, head_width),
                     functools.partial(lambda a, i: (0, a, head, 0, 0), a))
        for a in range(4)
    ]
    return pl.pallas_call(
        _kernel,
        grid=(1,),
        in_specs=specs,
        out_specs=[pl.BlockSpec((tokens_all, head_width), lambda i: (0, 0))] * 3,
        out_shape=(out, out, out),
        scratch_shapes=[
            pltpu.VMEM((tokens_all, BLOCK), jnp.float32),
            pltpu.VMEM((tokens_all, BLOCK), jnp.float32),
            pltpu.VMEM((tokens_all, head_width), jnp.float32),
            pltpu.VMEM((tokens_all, head_width), jnp.float32),
            pltpu.VMEM((head_width, tokens_all), jnp.bfloat16),
        ],
        compiler_params=pltpu.CompilerParams(vmem_limit_bytes=40 * 1024 * 1024),
    )(arrived, arrived, arrived, arrived)


def _gather_kernel(*refs, groups, per_dev, head_width):
    in_refs, out_ref = refs[:4], refs[4]
    for s in range(groups):
        for a, x_ref in enumerate(in_refs):
            for h in range(per_dev):
                col = (s * per_dev + h) * head_width
                out_ref[s, a, h] = x_ref[0, :, col:col + head_width]


def to_owners(inputs, page, seq_size, per_dev, head_width):
    page_count, tok_rows, feature_width = inputs[0].shape
    groups = max(1, seq_size // 2)
    while seq_size % groups:
        groups //= 2
    width = groups * per_dev * head_width
    in_spec = pl.BlockSpec((1, tok_rows, width), lambda g: (page, 0, g))
    out_spec = pl.BlockSpec((groups, 4, per_dev, tok_rows, head_width), lambda g: (g, 0, 0, 0, 0))
    return pl.pallas_call(
        functools.partial(_gather_kernel, groups=groups, per_dev=per_dev, head_width=head_width),
        grid=(seq_size // groups,),
        in_specs=[in_spec] * 4,
        out_specs=out_spec,
        out_shape=jax.ShapeDtypeStruct((seq_size, 4, per_dev, tok_rows, head_width), inputs[0].dtype),
    )(*inputs)


def _scatter_kernel(ret_ref, a_in, b_in, c_in, a_out, b_out, c_out, *, groups, per_dev, head_width):
    del a_in, b_in, c_in
    for s in range(groups):
        for a, o_ref in enumerate((a_out, b_out, c_out)):
            for h in range(per_dev):
                col = (s * per_dev + h) * head_width
                o_ref[0, :, col:col + head_width] = ret_ref[s, a, h]


def from_owners(returned, results, page, per_dev, head_width):
    seq_size = returned.shape[0]
    page_count, tok_rows, feature_width = results[0].shape
    groups = max(1, seq_size // 2)
    while seq_size % groups:
        groups //= 2
    width = groups * per_dev * head_width
    in_spec = pl.BlockSpec((groups, 3, per_dev, tok_rows, head_width), lambda g: (g, 0, 0, 0, 0))
    res_spec = pl.BlockSpec((1, tok_rows, width), lambda g: (page, 0, g))
    shape = jax.ShapeDtypeStruct(results[0].shape, results[0].dtype)
    return pl.pallas_call(
        functools.partial(_scatter_kernel, groups=groups, per_dev=per_dev, head_width=head_width),
        grid=(seq_size // groups,),
        in_specs=[in_spec, pl.BlockSpec(memory_space=pl.ANY)] + [pl.BlockSpec(memory_space=pl.ANY)] * 2,
        out_specs=[res_spec] * 3,
        out_shape=[shape] * 3,
        input_output_aliases={1: 0, 2: 1, 3: 2},
    )(returned, *results)


def exchange(x, seq_size):
    me = lax.axis_index("seq")
    out = x
    for shift in range(1, seq_size):
        piece = lax.dynamic_index_in_dim(x, (me + shift) % seq_size, 0)
        perm = [(i, (i + shift) % seq_size) for i in range(seq_size)]
        got = lax.ppermute(piece, "seq", perm)
        out = lax.dynamic_update_index_in_dim(out, got[0], (me - shift) % seq_size, 0)
    return out


def body(queries, key_vectors, value_vectors, out_grad):
    page_count, tok_rows, feature_width = queries.shape
    seq_size = lax.psum(1, "seq")
    head_width = feature_width // HEADS
    per_dev = HEADS // seq_size
    tokens_all = seq_size * tok_rows
    inputs = (queries, key_vectors, value_vectors, out_grad)
    results = tuple(jnp.zeros_like(queries) for _ in range(3))
    for page in range(page_count):
        part = to_owners(inputs, page, seq_size, per_dev, head_width)
        arrived = lax.all_to_all(part, "seq", split_axis=0, concat_axis=0, tiled=True)
        grads = []
        for head in range(per_dev):
            grads.append(jnp.stack(item_gradients(arrived, head)))
        grads = jnp.stack(grads).reshape(per_dev, 3, seq_size, tok_rows, head_width)
        grads = grads.transpose(2, 1, 0, 3, 4)
        if page == page_count - 1:
            returned = exchange(grads, seq_size)
        else:
            returned = lax.all_to_all(grads, "seq", split_axis=0, concat_axis=0, tiled=True)
        results = tuple(from_owners(returned, results, page, per_dev, head_width))
    return results


def solution(mesh):
    placed = P("group", "seq", None)
    return jax.shard_map(
        body,
        mesh=mesh,
        in_specs=(placed, placed, placed, placed),
        out_specs=(placed, placed, placed),
        check_vma=False,
    )
```
